128 devices in a mesh: dp: 4 (over x), tensor: 32 (over z, y, core).
Axes of the slice: x: 4, y: 4, z: 4, core: 2. Of those that a mesh axis runs over, the one named last changes fastest.
Arguments:
- inputs: bfloat16 [1024, 28672], P('dp', 'tensor'), may hold values from -0.1875 to 0.1875
- output_gradient: bfloat16 [1024, 8192], P('dp', 'tensor'), may hold values from -6 to 6
- frozen: bfloat16 [8192, 28672], P('dp', 'tensor'), may hold values from -0.5905695 to 0.5905695
- adapter_down_factor: bfloat16 [64, 28672], P(None, 'tensor'), may hold values from -0.03125 to 0.03125
- adapter_up_factor: bfloat16 [8192, 64], P('dp'), may hold values from -0.3125 to 0.3125
- magnitude: float32 [8192], P('dp'), may hold values from 0.5 to 2
Outputs:
- input_gradient_rows: bfloat16 [1024, 28672], P('dp', 'tensor')
- adapter_down_gradient: float32 [64, 28672], P(None, 'tensor')
- adapter_up_gradient: float32 [8192, 64], P('dp')
- magnitude_gradient: float32 [8192], P('dp')
The draws below stay inside these ranges and needn't reach their ends.
All inputs are finite; a program needn't handle non-finite values.
Results may differ from the reference program's by a relative error of at most 0.0057.
Values may be sent and summed in bfloat16 or wider, within the bound.
No kernel may reach another device: no remote copies, remote signals or barrier semaphores. Data moves between devices by JAX's collectives and lax.ppermute only.
A program may use at most 128 MiB of HBM per device.

```python
import math
import jax
import jax.numpy as jnp
from jax import lax

OUTPUT_WIDTH = 8192
INPUT_WIDTH = 28672
ADAPTER_RANK = 64
TOKENS = 1024
N_TENSOR = 32


def draw_frozen(key, part):
    base_key = jax.random.fold_in(key, 11)
    row_key, col_key, noise_key = jax.random.split(base_key, 3)
    row_scale = jnp.exp(jax.random.uniform(row_key, (OUTPUT_WIDTH, 1), jnp.float32) * math.log(10.0))
    col_scale = jnp.exp(jax.random.uniform(col_key, (1, INPUT_WIDTH), jnp.float32) * math.log(10.0))
    position = jnp.arange(INPUT_WIDTH, dtype=jnp.float32)[None, :] / INPUT_WIDTH
    noise = jax.random.truncated_normal(noise_key, -4.0, 4.0, (OUTPUT_WIDTH, INPUT_WIDTH), jnp.float32)
    trend = jnp.exp(position * math.log(3.0))
    values = noise * row_scale * col_scale * trend / (16.0 * math.sqrt(INPUT_WIDTH))
    return values.astype(jnp.bfloat16)


def levels(key, extent, cuts, least, top_value):
    loudness, own = 1.0, jax.random.fold_in(key, 6)
    for dim, shards_of in cuts:
        heights = jnp.exp(jax.random.uniform(jax.random.fold_in(own, dim), (shards_of,), jnp.float32, least / len(cuts), top_value / len(cuts)))
        loudness = loudness * jnp.repeat(heights, extent[dim] // shards_of).reshape([-1 if axis == dim else 1 for axis in range(len(extent))])
    return loudness


def normal_values(key, shape, deviation, most, cuts=(), kind=jnp.bfloat16):
    drawn = deviation * jax.random.normal(key, shape, jnp.float32)
    if cuts:
        drawn = drawn * levels(key, shape, cuts, -0.22, 0.18)
    return jnp.clip(drawn, -most, most).astype(kind)


def setup_inputs(seed: int = 0) -> dict:
    key_list = jax.random.split(jax.random.key(seed), 7)
    return {
        "inputs": normal_values(key_list[0], (TOKENS, INPUT_WIDTH), (TOKENS ** -0.5), 0.1875, ((0, 4), (1, 32))),
        "output_gradient": normal_values(key_list[1], (TOKENS, OUTPUT_WIDTH), 1.0, 6.0, ((0, 4), (1, 32))),
        "frozen": draw_frozen(jax.random.fold_in(key_list[6], 71), 0),
        "adapter_down_factor": normal_values(key_list[3], (ADAPTER_RANK, INPUT_WIDTH), INPUT_WIDTH ** -0.5, 0.03125, ((1, 32),)),
        "adapter_up_factor": normal_values(key_list[4], (OUTPUT_WIDTH, ADAPTER_RANK), 0.05, 0.3125, ((0, 4),)),
        "magnitude": jnp.clip(jnp.exp(math.log(2.0) - 1.3862944 * jax.random.uniform(key_list[5], (OUTPUT_WIDTH,), jnp.float32) ** levels(key_list[5], (OUTPUT_WIDTH,), ((0, 4),), -0.2, 0.2)), 0.5, 2.0),
    }


adapter_scale = 2.0
epsilon = 1e-06

def reference(inputs, output_gradient, frozen, adapter_down_factor, adapter_up_factor, magnitude):
    block_column_count = INPUT_WIDTH // N_TENSOR
    offsets = jnp.arange(N_TENSOR, dtype=jnp.int32) * block_column_count

    def merged_block(column_start):
        down_factor_block = lax.dynamic_slice_in_dim(adapter_down_factor, column_start, block_column_count, 1)
        weight_block_slice = lax.dynamic_slice_in_dim(frozen, column_start, block_column_count, 1)
        return weight_block_slice.astype(jnp.float32) + adapter_scale * jnp.dot(adapter_up_factor, down_factor_block, preferred_element_type=jnp.float32)

    def product_block(column_start):
        x_block = lax.dynamic_slice_in_dim(inputs, column_start, block_column_count, 1)
        return lax.dot_general(output_gradient, x_block, (((0,), (0,)), ((), ())), preferred_element_type=jnp.float32)

    def gather_stats(state_pair, column_start):
        squares, gradient_row_sums = state_pair
        combined_weight = merged_block(column_start)
        product = product_block(column_start)
        return ((squares + lax.optimization_barrier(jnp.sum(combined_weight * combined_weight, axis=1)), gradient_row_sums + lax.optimization_barrier(jnp.sum(product * combined_weight, axis=1))), None)
    initial = (jnp.zeros((OUTPUT_WIDTH,), jnp.float32), jnp.zeros((OUTPUT_WIDTH,), jnp.float32))
    (squares, gradient_row_sums), unused = lax.scan(gather_stats, initial, offsets)
    weight_row_norm = jnp.sqrt(squares + epsilon)
    col_scale = magnitude / weight_row_norm
    scaled_grad = (output_gradient.astype(jnp.float32) * col_scale[None, :]).astype(jnp.bfloat16)

    def make_grads(running, column_start):
        combined_weight = merged_block(column_start)
        product = product_block(column_start)
        combined_weight_gradient = col_scale[:, None] * product
        down_factor_gradient = adapter_scale * jnp.dot(adapter_up_factor.astype(jnp.float32).T, combined_weight_gradient, precision=lax.Precision.HIGHEST)
        down_factor_block = lax.dynamic_slice_in_dim(adapter_down_factor, column_start, block_column_count, 1)
        up_factor_piece = adapter_scale * jnp.dot(combined_weight_gradient, down_factor_block.astype(jnp.float32).T, precision=lax.Precision.HIGHEST)
        x_grad = jnp.dot(scaled_grad, combined_weight.astype(jnp.bfloat16), preferred_element_type=jnp.float32).astype(jnp.bfloat16)
        return (running + up_factor_piece, (x_grad, down_factor_gradient))
    up_factor_gradient, (x_blocks, down_factor_blocks) = lax.scan(make_grads, jnp.zeros((OUTPUT_WIDTH, ADAPTER_RANK), jnp.float32), offsets)
    input_gradient_rows = jnp.transpose(x_blocks, (1, 0, 2)).reshape(TOKENS, INPUT_WIDTH)
    adapter_down_gradient = jnp.transpose(down_factor_blocks, (1, 0, 2)).reshape(ADAPTER_RANK, INPUT_WIDTH)
    return (input_gradient_rows, adapter_down_gradient, up_factor_gradient, gradient_row_sums / weight_row_norm)
```

```python
import jax
import jax.numpy as jnp
from jax import lax
from jax.sharding import PartitionSpec as P

adapter_scale = 2.0
epsilon = 1e-06


def split_bf16(v):
    hi = v.astype(jnp.bfloat16)
    lo = (v - hi.astype(jnp.float32)).astype(jnp.bfloat16)
    return hi, lo


def dot2(spec, a, b_pair):
    hi, lo = b_pair
    return jnp.einsum(spec, a, hi, preferred_element_type=jnp.float32) + jnp.einsum(
        spec, a, lo, preferred_element_type=jnp.float32
    )


def transpose_pairs(n_dp, n_t):
    group = n_t // n_dp
    pairs = []
    for d in range(n_dp):
        for t in range(n_t):
            b, rest = divmod(t, group)
            pairs.append((d * n_t + t, b * n_t + d * group + rest))
    return pairs


def shift_pairs(n, k):
    return [(i, (i + k) % n) for i in range(n)]


def gather_dp(v, n_dp, d):
    out = jnp.zeros((n_dp,) + v.shape, v.dtype)
    out = lax.dynamic_update_index_in_dim(out, v, d, 0)
    for k in range(1, n_dp):
        piece = lax.ppermute(v, "dp", shift_pairs(n_dp, k))
        out = lax.dynamic_update_index_in_dim(out, piece, (d + n_dp - k) % n_dp, 0)
    return out


def reduce_scatter_dp(part, n_dp, d, axis):
    acc = lax.dynamic_index_in_dim(part, d, axis, keepdims=False)
    for k in range(1, n_dp):
        piece = lax.dynamic_index_in_dim(part, (d + k) % n_dp, axis, keepdims=False)
        piece = lax.ppermute(piece.astype(jnp.bfloat16), "dp", shift_pairs(n_dp, k))
        acc = acc + piece.astype(jnp.float32)
    return acc


def allreduce(v, axis, n):
    k = 1
    while k < n:
        v = v + lax.ppermute(v, axis, [(i, i ^ k) for i in range(n)])
        k *= 2
    return v


def make_local(n_dp, n_t):
    pairs = transpose_pairs(n_dp, n_t)

    def local(inputs, output_gradient, frozen, adapter_down_factor, adapter_up_factor, magnitude):
        d = lax.axis_index("dp")
        t = lax.axis_index("tensor")
        tok, cols = inputs.shape
        rows = frozen.shape[0]
        rank = adapter_down_factor.shape[0]

        og_p = lax.ppermute(output_gradient, ("dp", "tensor"), pairs)
        og_all = lax.all_gather(og_p, "tensor", axis=1, tiled=True).reshape(tok, n_dp, rows)
        x_all = gather_dp(inputs, n_dp, d)

        merged = frozen.astype(jnp.float32) + adapter_scale * jnp.dot(
            adapter_up_factor, adapter_down_factor, preferred_element_type=jnp.float32
        )
        merged_b = merged.astype(jnp.bfloat16)
        squares = jnp.sum(merged * merged, axis=1)
        h_local = jnp.dot(inputs, adapter_down_factor.T, preferred_element_type=jnp.float32)

        first = allreduce(jnp.concatenate([squares, h_local.reshape(-1)]), "tensor", n_t)
        total_squares = first[:rows]
        h_all = gather_dp(first[rows:].reshape(tok, rank), n_dp, d)

        weight_row_norm = jnp.sqrt(total_squares + epsilon)
        col_scale = magnitude / weight_row_norm

        scaled = (og_all.astype(jnp.float32) * col_scale).astype(jnp.bfloat16)
        ig_part = jnp.einsum("tbj,ji->bti", scaled, merged_b, preferred_element_type=jnp.float32)
        input_gradient_rows = reduce_scatter_dp(ig_part, n_dp, d, 0).astype(jnp.bfloat16)

        product = jnp.einsum("tbj,bti->ji", og_all, x_all, preferred_element_type=jnp.float32)
        grad_scale = allreduce(jnp.sum(product * merged, axis=1), "tensor", n_t)

        w = col_scale[:, None] * adapter_up_factor.astype(jnp.float32)
        g_all = allreduce(dot2("tbj,jr->btr", og_all, split_bf16(w)), "dp", n_dp)

        gh, gl = split_bf16(g_all)
        adapter_down_gradient = adapter_scale * (
            jnp.einsum("btr,bti->ri", gh, x_all, preferred_element_type=jnp.float32)
            + jnp.einsum("btr,bti->ri", gl, x_all, preferred_element_type=jnp.float32)
        )
        up = dot2("tbj,btr->jr", og_all, split_bf16(h_all))
        adapter_up_gradient = adapter_scale * (col_scale[:, None] * up)
        magnitude_gradient = grad_scale / weight_row_norm
        return (input_gradient_rows, adapter_down_gradient, adapter_up_gradient, magnitude_gradient)

    return local


def solution(mesh):
    n_dp = mesh.shape["dp"]
    n_t = mesh.shape["tensor"]
    placed = (
        P("dp", "tensor"),
        P("dp", "tensor"),
        P("dp", "tensor"),
        P(None, "tensor"),
        P("dp", None),
        P("dp"),
    )
    return jax.shard_map(
        make_local(n_dp, n_t),
        mesh=mesh,
        in_specs=placed,
        out_specs=(P("dp", "tensor"), P(None, "tensor"), P("dp", None), P("dp")),
        check_vma=False,
    )
```

```python
import jax
import jax.numpy as jnp
from jax import lax
from jax.sharding import PartitionSpec as P

adapter_scale = 2.0
epsilon = 1e-06


def split_bf16(v):
    hi = v.astype(jnp.bfloat16)
    lo = (v - hi.astype(jnp.float32)).astype(jnp.bfloat16)
    return hi, lo


def dot2(spec, a, b_pair):
    hi, lo = b_pair
    return jnp.einsum(spec, a, hi, preferred_element_type=jnp.float32) + jnp.einsum(
        spec, a, lo, preferred_element_type=jnp.float32
    )


def transpose_pairs(n_dp, n_t):
    group = n_t // n_dp
    pairs = []
    for d in range(n_dp):
        for t in range(n_t):
            b, rest = divmod(t, group)
            pairs.append((d * n_t + t, b * n_t + d * group + rest))
    return pairs


def shift_pairs(n, k):
    return [(i, (i + k) % n) for i in range(n)]


def gather_dp(v, n_dp, d):
    out = jnp.zeros((n_dp,) + v.shape, v.dtype)
    out = lax.dynamic_update_index_in_dim(out, v, d, 0)
    for k in range(1, n_dp):
        piece = lax.ppermute(v, "dp", shift_pairs(n_dp, k))
        out = lax.dynamic_update_index_in_dim(out, piece, (d + n_dp - k) % n_dp, 0)
    return out


def reduce_scatter_dp(part, n_dp, d, axis):
    acc = lax.dynamic_index_in_dim(part, d, axis, keepdims=False)
    for k in range(1, n_dp):
        piece = lax.dynamic_index_in_dim(part, (d + k) % n_dp, axis, keepdims=False)
        piece = lax.ppermute(piece.astype(jnp.bfloat16), "dp", shift_pairs(n_dp, k))
        acc = acc + piece.astype(jnp.float32)
    return acc


def allreduce(v, axis, n):
    k = 1
    while k < n:
        v = v + lax.ppermute(v, axis, [(i, i ^ k) for i in range(n)])
        k *= 2
    return v


def tensor_pairs(shape, move):
    nz, ny, nc = shape
    pairs = []
    for z in range(nz):
        for y in range(ny):
            for c in range(nc):
                dz, dy, dc = move(z, y, c)
                pairs.append(((z * ny + y) * nc + c, (dz * ny + dy) * nc + dc))
    return pairs


def gather_rows(og_p, shape, z, y, c):
    nz, ny, nc = shape
    tok, w = og_p.shape
    a = jnp.zeros((tok, ny * w), og_p.dtype)
    a = lax.dynamic_update_slice_in_dim(a, og_p, y * w, 1)
    for k in range(1, ny):
        piece = lax.ppermute(og_p, "tensor", tensor_pairs(shape, lambda zz, yy, cc: (zz, (yy + k) % ny, cc)))
        a = lax.dynamic_update_slice_in_dim(a, piece, ((y + ny - k) % ny) * w, 1)
    b = jnp.zeros((nz, tok, ny * w), og_p.dtype)
    b = lax.dynamic_update_index_in_dim(b, a, z, 0)
    for k in range(1, nz):
        piece = lax.ppermute(a, "tensor", tensor_pairs(shape, lambda zz, yy, cc: ((zz + k) % nz, yy, cc)))
        b = lax.dynamic_update_index_in_dim(b, piece, (z + nz - k) % nz, 0)
    out = jnp.zeros((nz, tok, nc, ny * w), og_p.dtype)
    out = lax.dynamic_update_index_in_dim(out, b, c, 2)
    for k in range(1, nc):
        piece = lax.ppermute(b, "tensor", tensor_pairs(shape, lambda zz, yy, cc: (zz, yy, (cc + k) % nc)))
        out = lax.dynamic_update_index_in_dim(out, piece, (c + nc - k) % nc, 2)
    return out.reshape(nz, tok, nc * ny * w)


def to_p(v, ny, nc):
    return v.reshape((ny, nc, -1) + v.shape[1:]).swapaxes(0, 1).reshape(v.shape)


def from_p(v, ny, nc):
    return v.reshape((nc, ny, -1) + v.shape[1:]).swapaxes(0, 1).reshape(v.shape)


def make_local(n_dp, n_t, tshape):
    pairs = transpose_pairs(n_dp, n_t)

    def local(inputs, output_gradient, frozen, adapter_down_factor, adapter_up_factor, magnitude):
        d = lax.axis_index("dp")
        t = lax.axis_index("tensor")
        tok, cols = inputs.shape
        rows = frozen.shape[0]
        rank = adapter_down_factor.shape[0]

        nz, ny, nc = tshape
        tz = t // (ny * nc)
        ty = (t // nc) % ny
        tc = t % nc

        og_p = lax.ppermute(output_gradient, ("dp", "tensor"), pairs)
        og_all = gather_rows(og_p, tshape, tz, ty, tc)
        x_all = gather_dp(inputs, n_dp, d)

        frozen_p = to_p(frozen, ny, nc)
        up_p = to_p(adapter_up_factor, ny, nc)
        magnitude_p = to_p(magnitude, ny, nc)
        merged = frozen_p.astype(jnp.float32) + adapter_scale * jnp.dot(
            up_p, adapter_down_factor, preferred_element_type=jnp.float32
        )
        merged_b = merged.astype(jnp.bfloat16)
        squares = jnp.sum(merged * merged, axis=1)
        h_local = jnp.dot(inputs, adapter_down_factor.T, preferred_element_type=jnp.float32)

        first = allreduce(jnp.concatenate([squares, h_local.reshape(-1)]), "tensor", n_t)
        total_squares = first[:rows]
        h_all = gather_dp(first[rows:].reshape(tok, rank), n_dp, d)

        weight_row_norm = jnp.sqrt(total_squares + epsilon)
        col_scale = magnitude_p / weight_row_norm

        scaled = (og_all.astype(jnp.float32) * col_scale).astype(jnp.bfloat16)
        ig_part = jnp.einsum("btj,ji->bti", scaled, merged_b, preferred_element_type=jnp.float32)
        own = lax.dynamic_index_in_dim(ig_part, d, 0, keepdims=False)
        sends = [
            lax.dynamic_index_in_dim(ig_part, (d + k) % n_dp, 0, keepdims=False).astype(jnp.bfloat16)
            for k in range(1, n_dp)
        ]
        sends, og_rest = lax.optimization_barrier((sends, og_all))
        acc = own
        for k in range(1, n_dp):
            acc = acc + lax.ppermute(sends[k - 1], "dp", shift_pairs(n_dp, k)).astype(jnp.float32)
        input_gradient_rows = acc.astype(jnp.bfloat16)

        product = jnp.einsum("btj,bti->ji", og_rest, x_all, preferred_element_type=jnp.float32)
        grad_scale = allreduce(jnp.sum(product * merged, axis=1), "tensor", n_t)

        w = col_scale[:, None] * up_p.astype(jnp.float32)
        g_all = allreduce(dot2("btj,jr->btr", og_rest, split_bf16(w)), "dp", n_dp)

        gh, gl = split_bf16(g_all)
        adapter_down_gradient = adapter_scale * (
            jnp.einsum("btr,bti->ri", gh, x_all, preferred_element_type=jnp.float32)
            + jnp.einsum("btr,bti->ri", gl, x_all, preferred_element_type=jnp.float32)
        )
        up = dot2("btj,btr->jr", og_rest, split_bf16(h_all))
        adapter_up_gradient = from_p(adapter_scale * (col_scale[:, None] * up), ny, nc)
        magnitude_gradient = from_p(grad_scale / weight_row_norm, ny, nc)
        return (input_gradient_rows, adapter_down_gradient, adapter_up_gradient, magnitude_gradient)

    return local


def solution(mesh):
    n_dp = mesh.shape["dp"]
    n_t = mesh.shape["tensor"]
    tshape = (n_dp, n_t // (2 * n_dp), 2)
    placed = (
        P("dp", "tensor"),
        P("dp", "tensor"),
        P("dp", "tensor"),
        P(None, "tensor"),
        P("dp", None),
        P("dp"),
    )
    return jax.shard_map(
        make_local(n_dp, n_t, tshape),
        mesh=mesh,
        in_specs=placed,
        out_specs=(P("dp", "tensor"), P(None, "tensor"), P("dp", None), P("dp")),
        check_vma=False,
    )
```

```python
import jax
import jax.numpy as jnp
from jax import lax
from jax.sharding import PartitionSpec as P

adapter_scale = 2.0
epsilon = 1e-06


def split_bf16(v):
    hi = v.astype(jnp.bfloat16)
    lo = (v - hi.astype(jnp.float32)).astype(jnp.bfloat16)
    return hi, lo


def dot2(spec, a, b_pair):
    hi, lo = b_pair
    return jnp.einsum(spec, a, hi, preferred_element_type=jnp.float32) + jnp.einsum(
        spec, a, lo, preferred_element_type=jnp.float32
    )


def transpose_pairs(n_dp, n_t):
    group = n_t // n_dp
    pairs = []
    for d in range(n_dp):
        for t in range(n_t):
            b, rest = divmod(t, group)
            pairs.append((d * n_t + t, b * n_t + d * group + rest))
    return pairs


def shift_pairs(n, k):
    return [(i, (i + k) % n) for i in range(n)]


def gather_dp(v, n_dp, d):
    out = jnp.zeros((n_dp,) + v.shape, v.dtype)
    out = lax.dynamic_update_index_in_dim(out, v, d, 0)
    for k in range(1, n_dp):
        piece = lax.ppermute(v, "dp", shift_pairs(n_dp, k))
        out = lax.dynamic_update_index_in_dim(out, piece, (d + n_dp - k) % n_dp, 0)
    return out


def reduce_scatter_dp(part, n_dp, d, axis):
    acc = lax.dynamic_index_in_dim(part, d, axis, keepdims=False)
    for k in range(1, n_dp):
        piece = lax.dynamic_index_in_dim(part, (d + k) % n_dp, axis, keepdims=False)
        piece = lax.ppermute(piece.astype(jnp.bfloat16), "dp", shift_pairs(n_dp, k))
        acc = acc + piece.astype(jnp.float32)
    return acc


def allreduce(v, axis, n):
    k = 1
    while k < n:
        v = v + lax.ppermute(v, axis, [(i, i ^ k) for i in range(n)])
        k *= 2
    return v


def tensor_pairs(shape, move):
    nz, ny, nc = shape
    pairs = []
    for z in range(nz):
        for y in range(ny):
            for c in range(nc):
                dz, dy, dc = move(z, y, c)
                pairs.append(((z * ny + y) * nc + c, (dz * ny + dy) * nc + dc))
    return pairs


def gather_rows(og_p, shape, z, y, c):
    nz, ny, nc = shape
    tok, w = og_p.shape
    a = jnp.zeros((tok, ny * w), og_p.dtype)
    a = lax.dynamic_update_slice_in_dim(a, og_p, y * w, 1)
    for k in range(1, ny):
        piece = lax.ppermute(og_p, "tensor", tensor_pairs(shape, lambda zz, yy, cc: (zz, (yy + k) % ny, cc)))
        a = lax.dynamic_update_slice_in_dim(a, piece, ((y + ny - k) % ny) * w, 1)
    b = jnp.zeros((nz, tok, ny * w), og_p.dtype)
    b = lax.dynamic_update_index_in_dim(b, a, z, 0)
    for k in range(1, nz):
        piece = lax.ppermute(a, "tensor", tensor_pairs(shape, lambda zz, yy, cc: ((zz + k) % nz, yy, cc)))
        b = lax.dynamic_update_index_in_dim(b, piece, (z + nz - k) % nz, 0)
    others = [
        lax.ppermute(b, "tensor", tensor_pairs(shape, lambda zz, yy, cc: (zz, yy, (cc + k) % nc)))
        for k in range(1, nc)
    ]
    blocks = []
    for yy in range(ny):
        for cc in range(nc):
            pick = b[:, :, yy * w : (yy + 1) * w]
            for k in range(1, nc):
                pick = jnp.where((c + nc - k) % nc == cc, others[k - 1][:, :, yy * w : (yy + 1) * w], pick)
            blocks.append(pick)
    return jnp.concatenate(blocks, axis=2)


def make_local(n_dp, n_t, tshape):
    pairs = transpose_pairs(n_dp, n_t)

    def local(inputs, output_gradient, frozen, adapter_down_factor, adapter_up_factor, magnitude):
        d = lax.axis_index("dp")
        t = lax.axis_index("tensor")
        tok, cols = inputs.shape
        rows = frozen.shape[0]
        rank = adapter_down_factor.shape[0]

        nz, ny, nc = tshape
        tz = t // (ny * nc)
        ty = (t // nc) % ny
        tc = t % nc

        og_p = lax.ppermute(output_gradient, ("dp", "tensor"), pairs)
        og_all = gather_rows(og_p, tshape, tz, ty, tc)
        x_all = gather_dp(inputs, n_dp, d)

        frozen_p = frozen
        up_p = adapter_up_factor
        magnitude_p = magnitude
        merged = frozen_p.astype(jnp.float32) + adapter_scale * jnp.dot(
            up_p, adapter_down_factor, preferred_element_type=jnp.float32
        )
        merged_b = merged.astype(jnp.bfloat16)
        squares = jnp.sum(merged * merged, axis=1)
        h_local = jnp.dot(inputs, adapter_down_factor.T, preferred_element_type=jnp.float32)

        first = allreduce(jnp.concatenate([squares, h_local.reshape(-1)]), "tensor", n_t)
        total_squares = first[:rows]
        h_all = gather_dp(first[rows:].reshape(tok, rank), n_dp, d)

        weight_row_norm = jnp.sqrt(total_squares + epsilon)
        col_scale = magnitude_p / weight_row_norm

        scaled = (og_all.astype(jnp.float32) * col_scale).astype(jnp.bfloat16)
        ig_part = jnp.einsum("btj,ji->bti", scaled, merged_b, preferred_element_type=jnp.float32)
        own = lax.dynamic_index_in_dim(ig_part, d, 0, keepdims=False)
        sends = [
            lax.dynamic_index_in_dim(ig_part, (d + k) % n_dp, 0, keepdims=False).astype(jnp.bfloat16)
            for k in range(1, n_dp)
        ]
        sends, og_rest = lax.optimization_barrier((sends, og_all))
        acc = own
        for k in range(1, n_dp):
            acc = acc + lax.ppermute(sends[k - 1], "dp", shift_pairs(n_dp, k)).astype(jnp.float32)
        input_gradient_rows = acc.astype(jnp.bfloat16)

        product = jnp.einsum("btj,bti->ji", og_rest, x_all, preferred_element_type=jnp.float32)
        grad_scale = allreduce(jnp.sum(product * merged, axis=1), "tensor", n_t)

        w = col_scale[:, None] * up_p.astype(jnp.float32)
        g_all = allreduce(dot2("btj,jr->btr", og_rest, split_bf16(w)), "dp", n_dp)

        gh, gl = split_bf16(g_all)
        adapter_down_gradient = adapter_scale * (
            jnp.einsum("btr,bti->ri", gh, x_all, preferred_element_type=jnp.float32)
            + jnp.einsum("btr,bti->ri", gl, x_all, preferred_element_type=jnp.float32)
        )
        up = dot2("btj,btr->jr", og_rest, split_bf16(h_all))
        adapter_up_gradient = adapter_scale * (col_scale[:, None] * up)
        magnitude_gradient = grad_scale / weight_row_norm
        return (input_gradient_rows, adapter_down_gradient, adapter_up_gradient, magnitude_gradient)

    return local


def solution(mesh):
    n_dp = mesh.shape["dp"]
    n_t = mesh.shape["tensor"]
    tshape = (n_dp, n_t // (2 * n_dp), 2)
    placed = (
        P("dp", "tensor"),
        P("dp", "tensor"),
        P("dp", "tensor"),
        P(None, "tensor"),
        P("dp", None),
        P("dp"),
    )
    return jax.shard_map(
        make_local(n_dp, n_t, tshape),
        mesh=mesh,
        in_specs=placed,
        out_specs=(P("dp", "tensor"), P(None, "tensor"), P("dp", None), P("dp")),
        check_vma=False,
    )
```

```python
import jax
import jax.numpy as jnp
from jax import lax
from jax.sharding import PartitionSpec as P


TENSOR = ("zy", "c")
adapter_scale = 2.0
epsilon = 1e-06


def split_bf16(v):
    hi = v.astype(jnp.bfloat16)
    lo = (v - hi.astype(jnp.float32)).astype(jnp.bfloat16)
    return hi, lo


def dot2(spec, a, b_pair):
    hi, lo = b_pair
    return jnp.einsum(spec, a, hi, preferred_element_type=jnp.float32) + jnp.einsum(
        spec, a, lo, preferred_element_type=jnp.float32
    )


def transpose_pairs(n_dp, n_t):
    group = n_t // n_dp
    pairs = []
    for d in range(n_dp):
        for t in range(n_t):
            b, rest = divmod(t, group)
            pairs.append((d * n_t + t, b * n_t + d * group + rest))
    return pairs


def shift_pairs(n, k):
    return [(i, (i + k) % n) for i in range(n)]


def gather_dp(v, n_dp, d):
    out = jnp.zeros((n_dp,) + v.shape, v.dtype)
    out = lax.dynamic_update_index_in_dim(out, v, d, 0)
    for k in range(1, n_dp):
        piece = lax.ppermute(v, "dp", shift_pairs(n_dp, k))
        out = lax.dynamic_update_index_in_dim(out, piece, (d + n_dp - k) % n_dp, 0)
    return out


def allreduce(v, axis, n):
    k = 1
    while k < n:
        v = v + lax.ppermute(v, axis, [(i, i ^ k) for i in range(n)])
        k *= 2
    return v


def make_local(n_dp, n_t):
    pairs = transpose_pairs(n_dp, n_t)

    def body(inputs, output_gradient, frozen, adapter_down_factor, adapter_up_factor, magnitude):
        d = lax.axis_index("dp")
        c = lax.axis_index("c")
        tok, _ = inputs.shape
        rows = frozen.shape[0]
        rank = adapter_down_factor.shape[0]

        og_p = lax.ppermute(output_gradient, ("dp",) + TENSOR, pairs)
        half = rows // 2
        og_c = lax.all_gather(og_p, "zy", axis=1, tiled=True).reshape(tok, n_dp, half)
        og_s = lax.ppermute(og_c, "c", [(0, 1), (1, 0)])
        x_all = gather_dp(inputs, n_dp, d)

        merged = frozen.astype(jnp.float32) + adapter_scale * jnp.dot(
            adapter_up_factor, adapter_down_factor, preferred_element_type=jnp.float32
        )
        merged_b = merged.astype(jnp.bfloat16)
        squares = jnp.sum(merged * merged, axis=1)
        h_local = jnp.dot(inputs, adapter_down_factor.T, preferred_element_type=jnp.float32)

        first = allreduce(jnp.concatenate([squares, h_local.reshape(-1)]), TENSOR, n_t)
        total_squares = first[:rows]
        h_all = gather_dp(first[rows:].reshape(tok, rank), n_dp, d)

        weight_row_norm = jnp.sqrt(total_squares + epsilon)
        col_scale = magnitude / weight_row_norm
        col_scale, weight_row_norm = lax.optimization_barrier((col_scale, weight_row_norm))

        def halves(v):
            v4 = v.reshape((-1, 2, rows // 8) + v.shape[1:])
            mine = lax.dynamic_index_in_dim(v4, c, 1, keepdims=False).reshape((half,) + v.shape[1:])
            other = lax.dynamic_index_in_dim(v4, 1 - c, 1, keepdims=False).reshape((half,) + v.shape[1:])
            return mine, other

        def join(mine, other):
            m4 = mine.reshape((-1, 1, rows // 8) + mine.shape[1:])
            o4 = other.reshape((-1, 1, rows // 8) + other.shape[1:])
            both = jnp.where(c == 0, jnp.concatenate([m4, o4], 1), jnp.concatenate([o4, m4], 1))
            return both.reshape((rows,) + mine.shape[1:])

        cs_c, cs_s = halves(col_scale)
        mb_c, mb_s = halves(merged_b)
        m_c, m_s = halves(merged)
        scaled_c = (og_c.astype(jnp.float32) * cs_c).astype(jnp.bfloat16)
        scaled_s = (og_s.astype(jnp.float32) * cs_s).astype(jnp.bfloat16)
        ig_part = jnp.einsum("tbj,ji->bti", scaled_c, mb_c, preferred_element_type=jnp.float32) + jnp.einsum(
            "tbj,ji->bti", scaled_s, mb_s, preferred_element_type=jnp.float32
        )
        own = lax.dynamic_index_in_dim(ig_part, d, 0, keepdims=False)
        sends = [
            lax.dynamic_index_in_dim(ig_part, (d + k) % n_dp, 0, keepdims=False).astype(jnp.bfloat16)
            for k in range(1, n_dp)
        ]
        acc = own
        received = [lax.ppermute(sends[k - 1], "dp", shift_pairs(n_dp, k)) for k in range(1, n_dp)]
        for piece in received:
            acc = acc + piece.astype(jnp.float32)
        input_gradient_rows = acc.astype(jnp.bfloat16)

        prod_c = jnp.einsum("tbj,bti->ji", og_c, x_all, preferred_element_type=jnp.float32)
        prod_s = jnp.einsum("tbj,bti->ji", og_s, x_all, preferred_element_type=jnp.float32)
        grad_scale_part = join(jnp.sum(prod_c * m_c, axis=1), jnp.sum(prod_s * m_s, axis=1))
        grad_scale = allreduce(grad_scale_part, TENSOR, n_t)

        w_c, w_s = halves(col_scale[:, None] * adapter_up_factor.astype(jnp.float32))
        g_all = allreduce(
            dot2("tbj,jr->btr", og_c, split_bf16(w_c)) + dot2("tbj,jr->btr", og_s, split_bf16(w_s)), "dp", n_dp
        )

        gh, gl = split_bf16(g_all)
        adapter_down_gradient = adapter_scale * (
            jnp.einsum("btr,bti->ri", gh, x_all, preferred_element_type=jnp.float32)
            + jnp.einsum("btr,bti->ri", gl, x_all, preferred_element_type=jnp.float32)
        )
        h_pair = split_bf16(h_all)
        up = join(dot2("tbj,btr->jr", og_c, h_pair), dot2("tbj,btr->jr", og_s, h_pair))
        adapter_up_gradient = adapter_scale * (col_scale[:, None] * up)
        magnitude_gradient = grad_scale / weight_row_norm
        return (input_gradient_rows, adapter_down_gradient, adapter_up_gradient, magnitude_gradient)

    return body


def solution(mesh):
    n_dp = mesh.shape["dp"]
    n_t = mesh.shape["tensor"]
    placed = (
        P("dp", TENSOR),
        P("dp", TENSOR),
        P("dp", TENSOR),
        P(None, TENSOR),
        P("dp", None),
        P("dp"),
    )
    fine = jax.sharding.Mesh(mesh.devices.reshape(n_dp, n_t // 2, 2), ("dp", "zy", "c"))
    return jax.shard_map(
        make_local(n_dp, n_t),
        mesh=fine,
        in_specs=placed,
        out_specs=(P("dp", TENSOR), P(None, TENSOR), P("dp", None), P("dp")),
        check_vma=False,
    )
```

```python
import jax
import jax.numpy as jnp
from jax import lax
from jax.sharding import PartitionSpec as P


adapter_scale = 2.0
epsilon = 1e-06


def split_bf16(v):
    hi = v.astype(jnp.bfloat16)
    lo = (v - hi.astype(jnp.float32)).astype(jnp.bfloat16)
    return hi, lo


def dot2(spec, a, b_pair):
    hi, lo = b_pair
    return jnp.einsum(spec, a, hi, preferred_element_type=jnp.float32) + jnp.einsum(
        spec, a, lo, preferred_element_type=jnp.float32
    )


def transpose_pairs(n_dp, n_t):
    group = n_t // n_dp
    pairs = []
    for d in range(n_dp):
        for t in range(n_t):
            b, rest = divmod(t, group)
            pairs.append((d * n_t + t, b * n_t + d * group + rest))
    return pairs


def shift_pairs(n, k):
    return [(i, (i + k) % n) for i in range(n)]


def gather_dp(v, n_dp, d):
    out = jnp.zeros((n_dp,) + v.shape, v.dtype)
    out = lax.dynamic_update_index_in_dim(out, v, d, 0)
    for k in range(1, n_dp):
        piece = lax.ppermute(v, "dp", shift_pairs(n_dp, k))
        out = lax.dynamic_update_index_in_dim(out, piece, (d + n_dp - k) % n_dp, 0)
    return out


def allreduce(v, axis, n):
    k = 1
    while k < n:
        v = v + lax.ppermute(v, axis, [(i, i ^ k) for i in range(n)])
        k *= 2
    return v


def make_local(n_dp, n_t):
    pairs = transpose_pairs(n_dp, n_t)

    def body(inputs, output_gradient, frozen, adapter_down_factor, adapter_up_factor, magnitude):
        d = lax.axis_index("dp")
        tok, _ = inputs.shape
        rows = frozen.shape[0]
        rank = adapter_down_factor.shape[0]

        og_p = lax.ppermute(output_gradient, ("dp", "tensor"), pairs)
        og_all = lax.all_gather(og_p, "tensor", axis=1, tiled=True).reshape(tok, n_dp, rows)
        x_all = gather_dp(inputs, n_dp, d)

        merged = frozen.astype(jnp.float32) + adapter_scale * jnp.dot(
            adapter_up_factor, adapter_down_factor, preferred_element_type=jnp.float32
        )
        merged_b = merged.astype(jnp.bfloat16)
        squares = jnp.sum(merged * merged, axis=1)
        h_local = jnp.dot(inputs, adapter_down_factor.T, preferred_element_type=jnp.float32)

        first = allreduce(jnp.concatenate([squares, h_local.reshape(-1)]), "tensor", n_t)
        total_squares = first[:rows]
        h_all = gather_dp(first[rows:].reshape(tok, rank), n_dp, d)

        weight_row_norm = jnp.sqrt(total_squares + epsilon)
        col_scale = magnitude / weight_row_norm
        col_scale, weight_row_norm = lax.optimization_barrier((col_scale, weight_row_norm))

        scaled = (og_all.astype(jnp.float32) * col_scale).astype(jnp.bfloat16)
        ig_part = jnp.einsum("tbj,ji->bti", scaled, merged_b, preferred_element_type=jnp.float32)
        own = lax.dynamic_index_in_dim(ig_part, d, 0, keepdims=False)
        sends = [
            lax.dynamic_index_in_dim(ig_part, (d + k) % n_dp, 0, keepdims=False).astype(jnp.bfloat16)
            for k in range(1, n_dp)
        ]
        acc = own
        received = [lax.ppermute(sends[k - 1], "dp", shift_pairs(n_dp, k)) for k in range(1, n_dp)]
        for piece in received:
            acc = acc + piece.astype(jnp.float32)
        input_gradient_rows = acc.astype(jnp.bfloat16)

        product = jnp.einsum("tbj,bti->ji", og_all, x_all, preferred_element_type=jnp.float32)
        grad_scale_part = jnp.sum(product * merged, axis=1)
        grad_scale = allreduce(grad_scale_part, "tensor", n_t)

        w = col_scale[:, None] * adapter_up_factor.astype(jnp.float32)
        g_all = allreduce(dot2("tbj,jr->btr", og_all, split_bf16(w)), "dp", n_dp)

        gh, gl = split_bf16(g_all)
        adapter_down_gradient = adapter_scale * (
            jnp.einsum("btr,bti->ri", gh, x_all, preferred_element_type=jnp.float32)
            + jnp.einsum("btr,bti->ri", gl, x_all, preferred_element_type=jnp.float32)
        )
        up = dot2("tbj,btr->jr", og_all, split_bf16(h_all))
        adapter_up_gradient = adapter_scale * (col_scale[:, None] * up)
        magnitude_gradient = grad_scale / weight_row_norm
        return (input_gradient_rows, adapter_down_gradient, adapter_up_gradient, magnitude_gradient)

    return body


def solution(mesh):
    n_dp = mesh.shape["dp"]
    n_t = mesh.shape["tensor"]
    placed = (
        P("dp", "tensor"),
        P("dp", "tensor"),
        P("dp", "tensor"),
        P(None, "tensor"),
        P("dp", None),
        P("dp"),
    )
    return jax.shard_map(
        make_local(n_dp, n_t),
        mesh=mesh,
        in_specs=placed,
        out_specs=(P("dp", "tensor"), P(None, "tensor"), P("dp", None), P("dp")),
        check_vma=False,
    )
```

```python
import jax
import jax.numpy as jnp
from jax import lax
from jax.sharding import PartitionSpec as P


adapter_scale = 2.0
epsilon = 1e-06


def split_bf16(v):
    hi = v.astype(jnp.bfloat16)
    lo = (v - hi.astype(jnp.float32)).astype(jnp.bfloat16)
    return hi, lo


def dot2(spec, a, b_pair):
    hi, lo = b_pair
    return jnp.einsum(spec, a, hi, preferred_element_type=jnp.float32) + jnp.einsum(
        spec, a, lo, preferred_element_type=jnp.float32
    )


def transpose_pairs(n_dp, n_t):
    group = n_t // n_dp
    pairs = []
    for d in range(n_dp):
        for t in range(n_t):
            b, rest = divmod(t, group)
            pairs.append((d * n_t + t, b * n_t + d * group + rest))
    return pairs


def shift_pairs(n, k):
    return [(i, (i + k) % n) for i in range(n)]


def gather_dp(v, n_dp, d):
    out = jnp.zeros((n_dp,) + v.shape, v.dtype)
    out = lax.dynamic_update_index_in_dim(out, v, d, 0)
    for k in range(1, n_dp):
        piece = lax.ppermute(v, "dp", shift_pairs(n_dp, k))
        out = lax.dynamic_update_index_in_dim(out, piece, (d + n_dp - k) % n_dp, 0)
    return out


def allreduce(v, axis, n):
    k = 1
    while k < n:
        v = v + lax.ppermute(v, axis, [(i, i ^ k) for i in range(n)])
        k *= 2
    return v


def make_local(n_dp, n_t):
    pairs = transpose_pairs(n_dp, n_t)

    def body(inputs, output_gradient, frozen, adapter_down_factor, adapter_up_factor, magnitude):
        d = lax.axis_index("dp")
        tok, _ = inputs.shape
        rows = frozen.shape[0]
        rank = adapter_down_factor.shape[0]

        og_p = lax.ppermute(output_gradient, ("dp", "tensor"), pairs)
        og_all = lax.all_gather(og_p, "tensor", axis=1, tiled=True).reshape(tok, n_dp, rows)
        x_all = gather_dp(inputs, n_dp, d)

        merged = frozen.astype(jnp.float32) + adapter_scale * jnp.dot(
            adapter_up_factor, adapter_down_factor, preferred_element_type=jnp.float32
        )
        merged_b = merged.astype(jnp.bfloat16)
        squares = jnp.sum(merged * merged, axis=1)
        h_local = jnp.dot(inputs, adapter_down_factor.T, preferred_element_type=jnp.float32)

        first = allreduce(jnp.concatenate([squares, h_local.reshape(-1)]), "tensor", n_t)
        total_squares = first[:rows]
        h_all = gather_dp(first[rows:].reshape(tok, rank), n_dp, d)

        weight_row_norm = jnp.sqrt(total_squares + epsilon)
        col_scale = magnitude / weight_row_norm
        col_scale, weight_row_norm = lax.optimization_barrier((col_scale, weight_row_norm))

        scaled = (og_all.astype(jnp.float32) * col_scale).astype(jnp.bfloat16)
        ig_part = jnp.einsum("tbj,ji->bti", scaled, merged_b, preferred_element_type=jnp.float32)
        own = lax.dynamic_index_in_dim(ig_part, d, 0, keepdims=False)
        sends = [
            lax.dynamic_index_in_dim(ig_part, (d + k) % n_dp, 0, keepdims=False).astype(jnp.bfloat16)
            for k in range(1, n_dp)
        ]
        acc = own
        received = [lax.ppermute(sends[k - 1], "dp", shift_pairs(n_dp, k)) for k in range(1, n_dp)]
        for piece in received:
            acc = acc + piece.astype(jnp.float32)
        input_gradient_rows = acc.astype(jnp.bfloat16)

        product = jnp.einsum("tbj,bti->ji", og_all, x_all, preferred_element_type=jnp.float32)
        grad_scale_part = jnp.sum(product * merged, axis=1)
        grad_scale = jnp.sum(lax.all_gather(grad_scale_part, "tensor"), axis=0)

        w = col_scale[:, None] * adapter_up_factor.astype(jnp.float32)
        g_part = dot2("tbj,jr->btr", og_all, split_bf16(w))
        g_all = allreduce(g_part, "dp", n_dp)

        gh, gl = split_bf16(g_all)
        adapter_down_gradient = adapter_scale * (
            jnp.einsum("btr,bti->ri", gh, x_all, preferred_element_type=jnp.float32)
            + jnp.einsum("btr,bti->ri", gl, x_all, preferred_element_type=jnp.float32)
        )
        up = dot2("tbj,btr->jr", og_all, split_bf16(h_all))
        adapter_up_gradient = adapter_scale * (col_scale[:, None] * up)
        magnitude_gradient = grad_scale / weight_row_norm
        return (input_gradient_rows, adapter_down_gradient, adapter_up_gradient, magnitude_gradient)

    return body


def solution(mesh):
    n_dp = mesh.shape["dp"]
    n_t = mesh.shape["tensor"]
    placed = (
        P("dp", "tensor"),
        P("dp", "tensor"),
        P("dp", "tensor"),
        P(None, "tensor"),
        P("dp", None),
        P("dp"),
    )
    return jax.shard_map(
        make_local(n_dp, n_t),
        mesh=mesh,
        in_specs=placed,
        out_specs=(P("dp", "tensor"), P(None, "tensor"), P("dp", None), P("dp")),
        check_vma=False,
    )
```

```python
import jax
import jax.numpy as jnp
from jax import lax
from jax.sharding import PartitionSpec as P


adapter_scale = 2.0
epsilon = 1e-06


def split_bf16(v):
    hi = v.astype(jnp.bfloat16)
    lo = (v - hi.astype(jnp.float32)).astype(jnp.bfloat16)
    return hi, lo


def dot2(spec, a, b_pair):
    hi, lo = b_pair
    return jnp.einsum(spec, a, hi, preferred_element_type=jnp.float32) + jnp.einsum(
        spec, a, lo, preferred_element_type=jnp.float32
    )


def transpose_pairs(n_dp, n_t):
    group = n_t // n_dp
    pairs = []
    for d in range(n_dp):
        for t in range(n_t):
            b, rest = divmod(t, group)
            pairs.append((d * n_t + t, b * n_t + d * group + rest))
    return pairs


def shift_pairs(n, k):
    return [(i, (i + k) % n) for i in range(n)]


def gather_dp(v, n_dp, d):
    out = jnp.zeros((n_dp,) + v.shape, v.dtype)
    out = lax.dynamic_update_index_in_dim(out, v, d, 0)
    for k in range(1, n_dp):
        piece = lax.ppermute(v, "dp", shift_pairs(n_dp, k))
        out = lax.dynamic_update_index_in_dim(out, piece, (d + n_dp - k) % n_dp, 0)
    return out


def allreduce(v, axis, n):
    k = 1
    while k < n:
        other = lax.ppermute(v, axis, [(i, i ^ k) for i in range(n)])
        v = v + other
        k *= 2
    return v


def make_local(n_dp, n_t):
    pairs = transpose_pairs(n_dp, n_t)

    def body(inputs, output_gradient, frozen, adapter_down_factor, adapter_up_factor, magnitude):
        d = lax.axis_index("dp")
        tok, _ = inputs.shape
        rows = frozen.shape[0]
        rank = adapter_down_factor.shape[0]

        og_p = lax.ppermute(output_gradient, ("dp", "tensor"), pairs)
        og_all = lax.all_gather(og_p, "tensor", axis=1, tiled=True).reshape(tok, n_dp, rows)
        x_all = gather_dp(inputs, n_dp, d)

        merged = frozen.astype(jnp.float32) + adapter_scale * jnp.dot(
            adapter_up_factor, adapter_down_factor, preferred_element_type=jnp.float32
        )
        merged_b = merged.astype(jnp.bfloat16)
        squares = jnp.sum(merged * merged, axis=1)
        h_local = jnp.dot(inputs, adapter_down_factor.T, preferred_element_type=jnp.float32)

        first = allreduce(jnp.concatenate([squares, h_local.reshape(-1)]), "tensor", n_t)
        total_squares = first[:rows]
        h_all = gather_dp(first[rows:].reshape(tok, rank), n_dp, d)

        weight_row_norm = jnp.sqrt(total_squares + epsilon)
        col_scale = magnitude / weight_row_norm
        col_scale, weight_row_norm = lax.optimization_barrier((col_scale, weight_row_norm))

        scaled = (og_all.astype(jnp.float32) * col_scale).astype(jnp.bfloat16)
        ig_part = jnp.einsum("tbj,ji->bti", scaled, merged_b, preferred_element_type=jnp.float32)
        own = lax.dynamic_index_in_dim(ig_part, d, 0, keepdims=False)
        sends = [
            lax.dynamic_index_in_dim(ig_part, (d + k) % n_dp, 0, keepdims=False).astype(jnp.bfloat16)
            for k in range(1, n_dp)
        ]
        acc = own
        received = [lax.ppermute(sends[k - 1], "dp", shift_pairs(n_dp, k)) for k in range(1, n_dp)]
        for piece in received:
            acc = acc + piece.astype(jnp.float32)
        input_gradient_rows = acc.astype(jnp.bfloat16)

        product = jnp.einsum("tbj,bti->ji", og_all, x_all, preferred_element_type=jnp.float32)
        grad_scale_part = jnp.sum(product * merged, axis=1)
        grad_scale = allreduce(grad_scale_part, "tensor", n_t)

        w = col_scale[:, None] * adapter_up_factor.astype(jnp.float32)
        g_part = dot2("tbj,jr->btr", og_all, split_bf16(w))
        g_all = allreduce(g_part, "dp", n_dp)

        gh, gl = split_bf16(g_all)
        adapter_down_gradient = adapter_scale * (
            jnp.einsum("btr,bti->ri", gh, x_all, preferred_element_type=jnp.float32)
            + jnp.einsum("btr,bti->ri", gl, x_all, preferred_element_type=jnp.float32)
        )
        up = dot2("tbj,btr->jr", og_all, split_bf16(h_all))
        adapter_up_gradient = adapter_scale * (col_scale[:, None] * up)
        magnitude_gradient = grad_scale / weight_row_norm
        return (input_gradient_rows, adapter_down_gradient, adapter_up_gradient, magnitude_gradient)

    return body


def solution(mesh):
    n_dp = mesh.shape["dp"]
    n_t = mesh.shape["tensor"]
    placed = (
        P("dp", "tensor"),
        P("dp", "tensor"),
        P("dp", "tensor"),
        P(None, "tensor"),
        P("dp", None),
        P("dp"),
    )
    return jax.shard_map(
        make_local(n_dp, n_t),
        mesh=mesh,
        in_specs=placed,
        out_specs=(P("dp", "tensor"), P(None, "tensor"), P("dp", None), P("dp")),
        check_vma=False,
    )
```

```python
import jax
import jax.numpy as jnp
from jax import lax
from jax.sharding import PartitionSpec as P


adapter_scale = 2.0
epsilon = 1e-06


def split_bf16(v):
    hi = v.astype(jnp.bfloat16)
    lo = (v - hi.astype(jnp.float32)).astype(jnp.bfloat16)
    return hi, lo


def dot2(spec, a, b_pair):
    hi, lo = b_pair
    return jnp.einsum(spec, a, hi, preferred_element_type=jnp.float32) + jnp.einsum(
        spec, a, lo, preferred_element_type=jnp.float32
    )


def transpose_pairs(n_dp, n_t):
    group = n_t // n_dp
    pairs = []
    for d in range(n_dp):
        for t in range(n_t):
            b, rest = divmod(t, group)
            pairs.append((d * n_t + t, b * n_t + d * group + rest))
    return pairs


def shift_pairs(n, k):
    return [(i, (i + k) % n) for i in range(n)]


def gather_dp(v, n_dp, d):
    out = jnp.zeros((n_dp,) + v.shape, v.dtype)
    out = lax.dynamic_update_index_in_dim(out, v, d, 0)
    for k in range(1, n_dp):
        piece = lax.ppermute(v, "dp", shift_pairs(n_dp, k))
        out = lax.dynamic_update_index_in_dim(out, piece, (d + n_dp - k) % n_dp, 0)
    return out


def allreduce(v, axis, n):
    k = 1
    while k < n:
        v = v + lax.ppermute(v, axis, [(i, i ^ k) for i in range(n)])
        k *= 2
    return v


def make_local(n_dp, n_t):
    pairs = transpose_pairs(n_dp, n_t)

    def body(inputs, output_gradient, frozen, adapter_down_factor, adapter_up_factor, magnitude):
        d = lax.axis_index("dp")
        tok, _ = inputs.shape
        rows = frozen.shape[0]
        rank = adapter_down_factor.shape[0]

        og_p = lax.ppermute(output_gradient, ("dp", "tensor"), pairs)
        og_all = lax.all_gather(og_p, "tensor", axis=1, tiled=True).reshape(tok, n_dp, rows)
        x_all = gather_dp(inputs, n_dp, d)

        merged = frozen.astype(jnp.float32) + adapter_scale * jnp.dot(
            adapter_up_factor, adapter_down_factor, preferred_element_type=jnp.float32
        )
        merged_b = merged.astype(jnp.bfloat16)
        squares = jnp.sum(merged * merged, axis=1)
        h_local = jnp.dot(inputs, adapter_down_factor.T, preferred_element_type=jnp.float32)

        first = allreduce(jnp.concatenate([squares, h_local.reshape(-1)]), "tensor", n_t)
        total_squares = first[:rows]
        h_all = gather_dp(first[rows:].reshape(tok, rank), n_dp, d)

        weight_row_norm = jnp.sqrt(total_squares + epsilon)
        col_scale = magnitude / weight_row_norm
        col_scale, weight_row_norm = lax.optimization_barrier((col_scale, weight_row_norm))

        scaled = (og_all.astype(jnp.float32) * col_scale).astype(jnp.bfloat16)

        def ig_for(group):
            block = lax.dynamic_index_in_dim(scaled, group, 1, keepdims=False)
            return jnp.dot(block, merged_b, preferred_element_type=jnp.float32)

        sends = [ig_for((d + k) % n_dp).astype(jnp.bfloat16) for k in range(1, n_dp)]
        own = ig_for(d)
        acc = own
        received = [lax.ppermute(sends[k - 1], "dp", shift_pairs(n_dp, k)) for k in range(1, n_dp)]
        for piece in received:
            acc = acc + piece.astype(jnp.float32)
        input_gradient_rows = acc.astype(jnp.bfloat16)

        product = jnp.einsum("tbj,bti->ji", og_all, x_all, preferred_element_type=jnp.float32)
        grad_scale_part = jnp.sum(product * merged, axis=1)
        grad_scale = allreduce(grad_scale_part, "tensor", n_t)

        w = col_scale[:, None] * adapter_up_factor.astype(jnp.float32)
        g_part = dot2("tbj,jr->btr", og_all, split_bf16(w))
        g_all = allreduce(g_part, "dp", n_dp)

        gh, gl = split_bf16(g_all)
        adapter_down_gradient = adapter_scale * (
            jnp.einsum("btr,bti->ri", gh, x_all, preferred_element_type=jnp.float32)
            + jnp.einsum("btr,bti->ri", gl, x_all, preferred_element_type=jnp.float32)
        )
        up = dot2("tbj,btr->jr", og_all, split_bf16(h_all))
        adapter_up_gradient = adapter_scale * (col_scale[:, None] * up)
        magnitude_gradient = grad_scale / weight_row_norm
        return (input_gradient_rows, adapter_down_gradient, adapter_up_gradient, magnitude_gradient)

    return body


def solution(mesh):
    n_dp = mesh.shape["dp"]
    n_t = mesh.shape["tensor"]
    placed = (
        P("dp", "tensor"),
        P("dp", "tensor"),
        P("dp", "tensor"),
        P(None, "tensor"),
        P("dp", None),
        P("dp"),
    )
    return jax.shard_map(
        make_local(n_dp, n_t),
        mesh=mesh,
        in_specs=placed,
        out_specs=(P("dp", "tensor"), P(None, "tensor"), P("dp", None), P("dp")),
        check_vma=False,
    )
```

```python
import jax
import jax.numpy as jnp
from jax import lax
from jax.sharding import PartitionSpec as P


adapter_scale = 2.0
epsilon = 1e-06


def split_bf16(v):
    hi = v.astype(jnp.bfloat16)
    lo = (v - hi.astype(jnp.float32)).astype(jnp.bfloat16)
    return hi, lo


def dot2(spec, a, b_pair):
    hi, lo = b_pair
    both = jnp.einsum(spec, a, jnp.concatenate([hi, lo], -1), preferred_element_type=jnp.float32)
    n = hi.shape[-1]
    return both[..., :n] + both[..., n:]


def transpose_pairs(n_dp, n_t):
    group = n_t // n_dp
    pairs = []
    for d in range(n_dp):
        for t in range(n_t):
            b, rest = divmod(t, group)
            pairs.append((d * n_t + t, b * n_t + d * group + rest))
    return pairs


def shift_pairs(n, k):
    return [(i, (i + k) % n) for i in range(n)]


def gather_dp(v, n_dp, d):
    out = jnp.zeros((n_dp,) + v.shape, v.dtype)
    out = lax.dynamic_update_index_in_dim(out, v, d, 0)
    for k in range(1, n_dp):
        piece = lax.ppermute(v, "dp", shift_pairs(n_dp, k))
        out = lax.dynamic_update_index_in_dim(out, piece, (d + n_dp - k) % n_dp, 0)
    return out


def allreduce(v, axis, n):
    k = 1
    while k < n:
        v = v + lax.ppermute(v, axis, [(i, i ^ k) for i in range(n)])
        k *= 2
    return v


def make_local(n_dp, n_t):
    pairs = transpose_pairs(n_dp, n_t)

    def body(inputs, output_gradient, frozen, adapter_down_factor, adapter_up_factor, magnitude):
        d = lax.axis_index("dp")
        tok, _ = inputs.shape
        rows = frozen.shape[0]
        rank = adapter_down_factor.shape[0]

        og_p = lax.ppermute(output_gradient, ("dp", "tensor"), pairs)
        og_all = lax.all_gather(og_p, "tensor", axis=1, tiled=True).reshape(tok, n_dp, rows)
        x_all = gather_dp(inputs, n_dp, d)

        merged = frozen.astype(jnp.float32) + adapter_scale * jnp.dot(
            adapter_up_factor, adapter_down_factor, preferred_element_type=jnp.float32
        )
        merged_b = merged.astype(jnp.bfloat16)
        squares = jnp.sum(merged * merged, axis=1)
        h_local = jnp.dot(inputs, adapter_down_factor.T, preferred_element_type=jnp.float32)

        first = allreduce(jnp.concatenate([squares, h_local.reshape(-1)]), "tensor", n_t)
        total_squares = first[:rows]
        h_all = gather_dp(first[rows:].reshape(tok, rank), n_dp, d)

        weight_row_norm = jnp.sqrt(total_squares + epsilon)
        col_scale = magnitude / weight_row_norm
        col_scale, weight_row_norm = lax.optimization_barrier((col_scale, weight_row_norm))

        scaled = (og_all.astype(jnp.float32) * col_scale).astype(jnp.bfloat16)

        def ig_for(group):
            block = lax.dynamic_index_in_dim(scaled, group, 1, keepdims=False)
            return jnp.dot(block, merged_b, preferred_element_type=jnp.float32)

        sends = [ig_for((d + k) % n_dp).astype(jnp.bfloat16) for k in range(1, n_dp)]
        own = ig_for(d)
        acc = own
        received = [lax.ppermute(sends[k - 1], "dp", shift_pairs(n_dp, k)) for k in range(1, n_dp)]
        for piece in received:
            acc = acc + piece.astype(jnp.float32)
        input_gradient_rows = acc.astype(jnp.bfloat16)

        product = jnp.einsum("tbj,bti->ji", og_all, x_all, preferred_element_type=jnp.float32)
        grad_scale_part = jnp.sum(product * merged, axis=1)
        grad_scale = allreduce(grad_scale_part, "tensor", n_t)

        w = col_scale[:, None] * adapter_up_factor.astype(jnp.float32)
        g_part = dot2("tbj,jr->btr", og_all, split_bf16(w))
        g_all = allreduce(g_part, "dp", n_dp)

        gh, gl = split_bf16(g_all)
        down = jnp.einsum("btr,bti->ri", jnp.concatenate([gh, gl], -1), x_all, preferred_element_type=jnp.float32)
        adapter_down_gradient = adapter_scale * (down[:rank] + down[rank:])
        up = dot2("tbj,btr->jr", og_all, split_bf16(h_all))
        adapter_up_gradient = adapter_scale * (col_scale[:, None] * up)
        magnitude_gradient = grad_scale / weight_row_norm
        return (input_gradient_rows, adapter_down_gradient, adapter_up_gradient, magnitude_gradient)

    return body


def solution(mesh):
    n_dp = mesh.shape["dp"]
    n_t = mesh.shape["tensor"]
    placed = (
        P("dp", "tensor"),
        P("dp", "tensor"),
        P("dp", "tensor"),
        P(None, "tensor"),
        P("dp", None),
        P("dp"),
    )
    return jax.shard_map(
        make_local(n_dp, n_t),
        mesh=mesh,
        in_specs=placed,
        out_specs=(P("dp", "tensor"), P(None, "tensor"), P("dp", None), P("dp")),
        check_vma=False,
    )
```

```python
import jax
import jax.numpy as jnp
from jax import lax
from jax.sharding import PartitionSpec as P


adapter_scale = 2.0
epsilon = 1e-06


def split_bf16(v):
    hi = v.astype(jnp.bfloat16)
    lo = (v - hi.astype(jnp.float32)).astype(jnp.bfloat16)
    return hi, lo


def dot2(spec, a, b_pair):
    hi, lo = b_pair
    both = jnp.einsum(spec, a, jnp.concatenate([hi, lo], -1), preferred_element_type=jnp.float32)
    n = hi.shape[-1]
    return both[..., :n] + both[..., n:]


def transpose_pairs(n_dp, n_t):
    group = n_t // n_dp
    pairs = []
    for d in range(n_dp):
        for t in range(n_t):
            b, rest = divmod(t, group)
            pairs.append((d * n_t + t, b * n_t + d * group + rest))
    return pairs


def shift_pairs(n, k):
    return [(i, (i + k) % n) for i in range(n)]


def gather_dp(v, n_dp, d):
    out = jnp.zeros((n_dp,) + v.shape, v.dtype)
    out = lax.dynamic_update_index_in_dim(out, v, d, 0)
    for k in range(1, n_dp):
        piece = lax.ppermute(v, "dp", shift_pairs(n_dp, k))
        out = lax.dynamic_update_index_in_dim(out, piece, (d + n_dp - k) % n_dp, 0)
    return out


def allreduce(v, axis, n):
    k = 1
    while k < n:
        v = v + lax.ppermute(v, axis, [(i, i ^ k) for i in range(n)])
        k *= 2
    return v


def allreduce_tensor(v, t, shape):
    nz, ny, nc = shape
    idx = lambda z, y, c: (z * ny + y) * nc + c
    v = v + lax.ppermute(v, "tensor", [(idx(z, y, c), idx(z, y, 1 - c)) for z in range(nz) for y in range(ny) for c in range(nc)])
    for size, coord, make in (
        (ny, (t // nc) % ny, lambda k: [(idx(z, y, c), idx(z, (y + k) % ny, c)) for z in range(nz) for y in range(ny) for c in range(nc)]),
        (nz, t // (ny * nc), lambda k: [(idx(z, y, c), idx((z + k) % nz, y, c)) for z in range(nz) for y in range(ny) for c in range(nc)]),
    ):
        slots = jnp.zeros((size,) + v.shape, v.dtype)
        slots = lax.dynamic_update_index_in_dim(slots, v, coord, 0)
        for k in range(1, size):
            slots = lax.dynamic_update_index_in_dim(slots, lax.ppermute(v, "tensor", make(k)), (coord + size - k) % size, 0)
        v = slots[0]
        for i in range(1, size):
            v = v + slots[i]
    return v


def make_local(n_dp, n_t):
    pairs = transpose_pairs(n_dp, n_t)

    def body(inputs, output_gradient, frozen, adapter_down_factor, adapter_up_factor, magnitude):
        d = lax.axis_index("dp")
        t = lax.axis_index("tensor")
        tok, _ = inputs.shape
        rows = frozen.shape[0]
        rank = adapter_down_factor.shape[0]

        og_p = lax.ppermute(output_gradient, ("dp", "tensor"), pairs)
        og_all = lax.all_gather(og_p, "tensor", axis=1, tiled=True).reshape(tok, n_dp, rows)
        x_all = gather_dp(inputs, n_dp, d)

        merged = frozen.astype(jnp.float32) + adapter_scale * jnp.dot(
            adapter_up_factor, adapter_down_factor, preferred_element_type=jnp.float32
        )
        merged_b = merged.astype(jnp.bfloat16)
        squares = jnp.sum(merged * merged, axis=1)
        h_local = jnp.dot(inputs, adapter_down_factor.T, preferred_element_type=jnp.float32)

        first = allreduce(jnp.concatenate([squares, h_local.reshape(-1)]), "tensor", n_t)
        total_squares = first[:rows]
        h_all = gather_dp(first[rows:].reshape(tok, rank), n_dp, d)

        weight_row_norm = jnp.sqrt(total_squares + epsilon)
        col_scale = magnitude / weight_row_norm
        col_scale, weight_row_norm = lax.optimization_barrier((col_scale, weight_row_norm))

        scaled = (og_all.astype(jnp.float32) * col_scale).astype(jnp.bfloat16)

        def ig_for(group):
            block = lax.dynamic_index_in_dim(scaled, group, 1, keepdims=False)
            return jnp.dot(block, merged_b, preferred_element_type=jnp.float32)

        sends = [ig_for((d + k) % n_dp).astype(jnp.bfloat16) for k in range(1, n_dp)]
        own = ig_for(d)
        acc = own
        received = [lax.ppermute(sends[k - 1], "dp", shift_pairs(n_dp, k)) for k in range(1, n_dp)]
        for piece in received:
            acc = acc + piece.astype(jnp.float32)
        input_gradient_rows = acc.astype(jnp.bfloat16)

        product = jnp.einsum("tbj,bti->ji", og_all, x_all, preferred_element_type=jnp.float32)
        grad_scale_part = jnp.sum(product * merged, axis=1)
        grad_scale = allreduce_tensor(grad_scale_part, t, (n_dp, n_t // (2 * n_dp), 2))

        w = col_scale[:, None] * adapter_up_factor.astype(jnp.float32)
        g_part = dot2("tbj,jr->btr", og_all, split_bf16(w))
        g_all = allreduce(g_part, "dp", n_dp)

        gh, gl = split_bf16(g_all)
        down = jnp.einsum("btr,bti->ri", jnp.concatenate([gh, gl], -1), x_all, preferred_element_type=jnp.float32)
        adapter_down_gradient = adapter_scale * (down[:rank] + down[rank:])
        up = dot2("tbj,btr->jr", og_all, split_bf16(h_all))
        adapter_up_gradient = adapter_scale * (col_scale[:, None] * up)
        magnitude_gradient = grad_scale / weight_row_norm
        return (input_gradient_rows, adapter_down_gradient, adapter_up_gradient, magnitude_gradient)

    return body


def solution(mesh):
    n_dp = mesh.shape["dp"]
    n_t = mesh.shape["tensor"]
    placed = (
        P("dp", "tensor"),
        P("dp", "tensor"),
        P("dp", "tensor"),
        P(None, "tensor"),
        P("dp", None),
        P("dp"),
    )
    return jax.shard_map(
        make_local(n_dp, n_t),
        mesh=mesh,
        in_specs=placed,
        out_specs=(P("dp", "tensor"), P(None, "tensor"), P("dp", None), P("dp")),
        check_vma=False,
    )
```

```python
import jax
import jax.numpy as jnp
from jax import lax
from jax.sharding import PartitionSpec as P


adapter_scale = 2.0
epsilon = 1e-06


def split_bf16(v):
    hi = v.astype(jnp.bfloat16)
    lo = (v - hi.astype(jnp.float32)).astype(jnp.bfloat16)
    return hi, lo


def dot2(spec, a, b_pair):
    hi, lo = b_pair
    both = jnp.einsum(spec, a, jnp.concatenate([hi, lo], -1), preferred_element_type=jnp.float32)
    n = hi.shape[-1]
    return both[..., :n] + both[..., n:]


def transpose_pairs(n_dp, n_t):
    group = n_t // n_dp
    pairs = []
    for d in range(n_dp):
        for t in range(n_t):
            b, rest = divmod(t, group)
            pairs.append((d * n_t + t, b * n_t + d * group + rest))
    return pairs


def shift_pairs(n, k):
    return [(i, (i + k) % n) for i in range(n)]


def gather_dp(v, n_dp, d):
    out = jnp.zeros((n_dp,) + v.shape, v.dtype)
    out = lax.dynamic_update_index_in_dim(out, v, d, 0)
    for k in range(1, n_dp):
        piece = lax.ppermute(v, "dp", shift_pairs(n_dp, k))
        out = lax.dynamic_update_index_in_dim(out, piece, (d + n_dp - k) % n_dp, 0)
    return out


def allreduce(v, axis, n):
    k = 1
    while k < n:
        v = v + lax.ppermute(v, axis, [(i, i ^ k) for i in range(n)])
        k *= 2
    return v


def make_local(n_dp, n_t):
    pairs = transpose_pairs(n_dp, n_t)

    def body(inputs, output_gradient, frozen, adapter_down_factor, adapter_up_factor, magnitude):
        d = lax.axis_index("dp")
        tok, _ = inputs.shape
        rows = frozen.shape[0]
        rank = adapter_down_factor.shape[0]

        og_p = lax.ppermute(output_gradient, ("dp", "tensor"), pairs)
        og_all = lax.all_gather(og_p, "tensor", axis=1, tiled=True).reshape(tok, n_dp, rows)
        x_all = gather_dp(inputs, n_dp, d)

        merged = frozen.astype(jnp.float32) + adapter_scale * jnp.dot(
            adapter_up_factor, adapter_down_factor, preferred_element_type=jnp.float32
        )
        merged_b = merged.astype(jnp.bfloat16)
        squares = jnp.sum(merged * merged, axis=1)
        h_local = jnp.dot(inputs, adapter_down_factor.T, preferred_element_type=jnp.float32)

        total_squares = allreduce(squares, "tensor", n_t)
        h_sum = allreduce(h_local, "tensor", n_t)
        h_all = gather_dp(h_sum, n_dp, d)

        weight_row_norm = jnp.sqrt(total_squares + epsilon)
        col_scale = magnitude / weight_row_norm
        col_scale, weight_row_norm = lax.optimization_barrier((col_scale, weight_row_norm))

        scaled = (og_all.astype(jnp.float32) * col_scale).astype(jnp.bfloat16)

        def ig_for(group):
            block = lax.dynamic_index_in_dim(scaled, group, 1, keepdims=False)
            return jnp.dot(block, merged_b, preferred_element_type=jnp.float32)

        sends = [ig_for((d + k) % n_dp).astype(jnp.bfloat16) for k in range(1, n_dp)]
        own = ig_for(d)
        acc = own
        received = [lax.ppermute(sends[k - 1], "dp", shift_pairs(n_dp, k)) for k in range(1, n_dp)]
        for piece in received:
            acc = acc + piece.astype(jnp.float32)
        input_gradient_rows = acc.astype(jnp.bfloat16)

        product = jnp.einsum("tbj,bti->ji", og_all, x_all, preferred_element_type=jnp.float32)
        grad_scale_part = jnp.sum(product * merged, axis=1)
        grad_scale = allreduce(grad_scale_part, "tensor", n_t)

        w = col_scale[:, None] * adapter_up_factor.astype(jnp.float32)
        g_part = dot2("tbj,jr->btr", og_all, split_bf16(w))
        g_all = allreduce(g_part, "dp", n_dp)

        gh, gl = split_bf16(g_all)
        down = jnp.einsum("btr,bti->ri", jnp.concatenate([gh, gl], -1), x_all, preferred_element_type=jnp.float32)
        adapter_down_gradient = adapter_scale * (down[:rank] + down[rank:])
        up = dot2("tbj,btr->jr", og_all, split_bf16(h_all))
        adapter_up_gradient = adapter_scale * (col_scale[:, None] * up)
        magnitude_gradient = grad_scale / weight_row_norm
        return (input_gradient_rows, adapter_down_gradient, adapter_up_gradient, magnitude_gradient)

    return body


def solution(mesh):
    n_dp = mesh.shape["dp"]
    n_t = mesh.shape["tensor"]
    placed = (
        P("dp", "tensor"),
        P("dp", "tensor"),
        P("dp", "tensor"),
        P(None, "tensor"),
        P("dp", None),
        P("dp"),
    )
    return jax.shard_map(
        make_local(n_dp, n_t),
        mesh=mesh,
        in_specs=placed,
        out_specs=(P("dp", "tensor"), P(None, "tensor"), P("dp", None), P("dp")),
        check_vma=False,
    )
```
